32 devices in a mesh: group: 2 (over y), tm: 4 (over z), member: 2 (over x), sub: 2 (over core).
Axes of the slice: x: 2, y: 2, z: 4, core: 2. Of those that a mesh axis runs over, the one named last changes fastest.
Arguments:
- slices: float32 [8, 4, 2, 256, 256], P(('group', 'member', 'sub'), 'tm'), parts along dimension 0, may hold values from -1 to 1, as said below
- controls: float32 [4, 2, 256, 256], replicated, as said below
- target: float32 [4, 256, 256], P('group'), parts along dimension 0, may hold values from -1 to 1, as said below
Outputs:
- gradient: float32 [8, 4], P(('group', 'tm')), parts along dimension 0
The draws below stay inside these ranges and needn't reach their ends.
There are 2 independent parts, one for each index of `group`. The reference program is written for one: setup_inputs(seed, part) draws one part's arguments, and reference() takes and returns one part's arrays. A program takes and returns all parts, laid end to end along the dimension named above; an argument that names none is the same for every part. Nothing has to cross between parts.
Inputs may be any that keep to these rules, and one draw needn't show every extreme that they name: Each slices[m, k] is a unitary matrix. `controls`: each control generator is Hermitian. The target is a unitary matrix.
All inputs are finite; a program needn't handle non-finite values.
Results may differ from the reference program's by a relative error of at most 0.0003.
Values sent between devices are 32-bit elements; how exact they have to be, the bound alone decides.
No kernel may reach another device: no remote copies, remote signals or barrier semaphores. Data moves between devices by JAX's collectives and lax.ppermute only.
A program may use at most 64 MiB of HBM per device.

```python
import math
import jax
import jax.numpy as jnp
from jax import lax

N = 256
NCTRL = 4
TIME = 4
MEMBERS = 4


def cayley_unitary(key, scale):
    key_a, key_b = jax.random.split(key)
    first = jax.random.normal(key_a, (N, N), jnp.float32)
    second = jax.random.normal(key_b, (N, N), jnp.float32)
    factor = scale / (2.0 * math.sqrt(N))
    symmetric = (first + first.T) * factor
    antisym = (second - second.T) * factor
    unit = jnp.eye(N, dtype=jnp.float32)
    left_re = unit - antisym
    block = jnp.concatenate([jnp.concatenate([left_re, -symmetric], 1), jnp.concatenate([symmetric, left_re], 1)], 0)
    rhs = jnp.concatenate([unit + antisym, -symmetric], 0)
    solved = jnp.linalg.solve(block, rhs)
    return jnp.stack([solved[:N], solved[N:]])


def draw_slices(key, part):
    scale = 1.0
    keys = jax.random.split(key, MEMBERS * TIME)
    mats = lax.map(lambda item: cayley_unitary(item, scale), keys)
    return mats.reshape((MEMBERS, TIME, 2, N, N))


def draw_target(key, part):
    return cayley_unitary(jax.random.fold_in(key, 7), 1.0)


def draw_controls(key, part):
    key_a, key_b = jax.random.split(jax.random.fold_in(key, 11), 2)
    first = jax.random.normal(key_a, (NCTRL, N, N), jnp.float32)
    second = jax.random.normal(key_b, (NCTRL, N, N), jnp.float32)
    factor = 1.0 / math.sqrt(2.0 * N)
    real_part = (first + jnp.swapaxes(first, 1, 2)) * factor
    imag_part = (second - jnp.swapaxes(second, 1, 2)) * factor
    gens = jnp.stack([real_part, imag_part], axis=1)
    return gens


def setup_inputs(seed: int = 0, part: int = 0) -> dict:
    splits = jax.random.split(jax.random.key(seed), 4)
    part_keys = jax.random.split(jax.random.fold_in(splits[3], part), 4)
    return {
        "slices": draw_slices(jax.random.fold_in(jax.random.fold_in(splits[3], part), 71), part),
        "controls": draw_controls(jax.random.fold_in(splits[3], 71), part),
        "target": draw_target(jax.random.fold_in(jax.random.fold_in(splits[3], part), 71), part),
    }


HIGH = lax.Precision.HIGHEST

def cmul(left, right):
    real_part = jnp.matmul(left[..., 0, :, :], right[..., 0, :, :], precision=HIGH) - jnp.matmul(left[..., 1, :, :], right[..., 1, :, :], precision=HIGH)
    imag_part = jnp.matmul(left[..., 0, :, :], right[..., 1, :, :], precision=HIGH) + jnp.matmul(left[..., 1, :, :], right[..., 0, :, :], precision=HIGH)
    return jnp.stack([real_part, imag_part], axis=-3)

def cdagger(matrix):
    return jnp.stack([jnp.swapaxes(matrix[..., 0, :, :], -1, -2), -jnp.swapaxes(matrix[..., 1, :, :], -1, -2)], axis=-3)

def reference(slices, controls, target):
    order = target.shape[-1]
    identity = jnp.stack([jnp.eye(order, dtype=jnp.float32), jnp.zeros((order, order), jnp.float32)])
    target_dag = cdagger(target)

    def one_member(member_slices):

        def forward_step(carry, unit):
            result = cmul(unit, carry)
            return (result, result)
        whole, forward = lax.scan(forward_step, identity, member_slices)

        def backward_step(carry, unit):
            return (cmul(carry, unit), carry)
        _, backward = lax.scan(backward_step, identity, member_slices, reverse=True)
        correlation_mat = cmul(target_dag, whole)
        over_re = jnp.trace(correlation_mat[0])
        over_im = jnp.trace(correlation_mat[1])
        costate = cmul(cmul(forward, target_dag[None]), backward)
        s_re = jnp.einsum('kab,jab->kj', costate[:, 0], controls[:, 0], precision=HIGH) + jnp.einsum('kab,jab->kj', costate[:, 1], controls[:, 1], precision=HIGH)
        s_im = jnp.einsum('kab,jab->kj', costate[:, 1], controls[:, 0], precision=HIGH) - jnp.einsum('kab,jab->kj', costate[:, 0], controls[:, 1], precision=HIGH)
        return over_re * s_im - over_im * s_re
    terms = lax.map(one_member, slices)
    return jnp.sum(terms, axis=0) * (2.0 / MEMBERS)
```

```python
import jax
import jax.numpy as jnp
from jax import lax
from jax.sharding import PartitionSpec as P

HIGH = lax.Precision.HIGHEST
CHUNKS = 4


def block_left(u):
    top = jnp.concatenate([u[:, 0], -u[:, 1]], axis=-1)
    bottom = jnp.concatenate([u[:, 1], u[:, 0]], axis=-1)
    return jnp.concatenate([top, bottom], axis=-2)


def block_right(u):
    top = jnp.concatenate([u[:, 0], u[:, 1]], axis=-1)
    bottom = jnp.concatenate([-u[:, 1], u[:, 0]], axis=-1)
    return jnp.concatenate([top, bottom], axis=-2)


def per_device(slices, controls, target):
    members_here = slices.shape[0]
    order = slices.shape[-1]
    chunks = CHUNKS
    width = order // chunks
    blocks = lax.axis_size("tm")
    position = lax.axis_index("tm")
    unit = slices[:, 0]
    left_op = block_left(unit)
    right_op = block_right(unit)
    target_dag = jnp.concatenate([target[0].T, -target[1].T], axis=-1)
    right_pairs = [(i, i + 1) for i in range(blocks - 1)]
    left_pairs = [(i + 1, i) for i in range(blocks - 1)]
    is_first = position == 0
    is_last = position == blocks - 1

    fwd_buf = jnp.zeros((chunks + 2, members_here, 2 * order, width), jnp.float32)
    bwd_buf = jnp.zeros((chunks + 2, members_here, width, 2 * order), jnp.float32)
    fwd_out = None
    bwd_out = None
    steps = chunks + blocks - 1
    for step in range(steps):
        if step == 0:
            fwd_in = jnp.zeros((members_here, 2 * order, width), jnp.float32)
            bwd_in = jnp.zeros((members_here, width, 2 * order), jnp.float32)
        else:
            fwd_in = lax.ppermute(fwd_out, "tm", right_pairs)
            bwd_in = lax.ppermute(bwd_out, "tm", left_pairs)
        if step < chunks:
            cols = slice(step * width, (step + 1) * width)
            own_cols = jnp.concatenate([unit[:, 0, :, cols], unit[:, 1, :, cols]], axis=-2)
            rows = jnp.broadcast_to(target_dag[None, step * width:(step + 1) * width], bwd_in.shape)
            fwd_new = jnp.where(
                is_first, own_cols,
                jnp.einsum("mab,mbw->maw", left_op, fwd_in, precision=HIGH),
            )
            bwd_in = jnp.where(is_last, rows, bwd_in)
        else:
            fwd_new = jnp.einsum("mab,mbw->maw", left_op, fwd_in, precision=HIGH)
        fwd_chunk = jnp.clip(step - position, -1, chunks) + 1
        bwd_chunk = jnp.clip(step - (blocks - 1 - position), -1, chunks) + 1
        fwd_buf = lax.dynamic_update_index_in_dim(fwd_buf, fwd_new, fwd_chunk, 0)
        bwd_buf = lax.dynamic_update_index_in_dim(bwd_buf, bwd_in, bwd_chunk, 0)
        fwd_out = fwd_new
        if step < steps - 1:
            bwd_out = jnp.einsum("mwa,mab->mwb", bwd_in, right_op, precision=HIGH)

    fwd_all = fwd_buf[1:chunks + 1].reshape(chunks, members_here, 2, order, width)
    bwd_all = bwd_buf[1:chunks + 1].reshape(chunks, members_here, width, 2, order)
    parts = jnp.einsum("cmpaw,cmwqb->mpqab", fwd_all, bwd_all, precision=HIGH)
    q_re = parts[:, 0, 0] - parts[:, 1, 1]
    q_im = parts[:, 0, 1] + parts[:, 1, 0]
    eye = jnp.eye(order, dtype=bool)
    over_re = jnp.sum(jnp.where(eye, q_re, 0.0), axis=(-2, -1))
    over_im = jnp.sum(jnp.where(eye, q_im, 0.0), axis=(-2, -1))
    h_re = controls[None, :, 0]
    h_im = controls[None, :, 1]
    s_re = jnp.sum(q_re[:, None] * h_re + q_im[:, None] * h_im, axis=(-2, -1))
    s_im = jnp.sum(q_im[:, None] * h_re - q_re[:, None] * h_im, axis=(-2, -1))
    terms = over_re[:, None] * s_im - over_im[:, None] * s_re
    partial_value = jnp.sum(terms, axis=0, keepdims=True)
    total = lax.psum(partial_value, ("member", "sub"))
    member_count = members_here * lax.axis_size("member") * lax.axis_size("sub")
    return total * (2.0 / member_count)


def solution(mesh):
    placed = (P(("group", "member", "sub"), "tm", None, None, None), P(), P("group", None, None))
    return jax.shard_map(
        per_device, mesh=mesh, in_specs=placed, out_specs=P(("group", "tm"), None), check_vma=False
    )
```

```python
import jax
import jax.numpy as jnp
from jax import lax
from jax.sharding import PartitionSpec as P

HIGH = lax.Precision.HIGH
CHUNKS = 4


def block_left(u):
    top = jnp.concatenate([u[:, 0], -u[:, 1]], axis=-1)
    bottom = jnp.concatenate([u[:, 1], u[:, 0]], axis=-1)
    return jnp.concatenate([top, bottom], axis=-2)


def block_right(u):
    top = jnp.concatenate([u[:, 0], u[:, 1]], axis=-1)
    bottom = jnp.concatenate([-u[:, 1], u[:, 0]], axis=-1)
    return jnp.concatenate([top, bottom], axis=-2)


def butterfly_sum(value, axes):
    for axis in axes:
        size = lax.axis_size(axis)
        if size & (size - 1):
            value = lax.psum(value, axis)
            continue
        distance = 1
        while distance < size:
            pairs = [(i, i ^ distance) for i in range(size)]
            value = value + lax.ppermute(value, axis, pairs)
            distance *= 2
    return value


def per_device(slices, controls, target):
    members_here = slices.shape[0]
    order = slices.shape[-1]
    chunks = CHUNKS
    width = order // chunks
    blocks = lax.axis_size("tm")
    position = lax.axis_index("tm")
    unit = slices[:, 0]
    left_op = block_left(unit)
    right_op = block_right(unit)
    target_dag = jnp.concatenate([target[0].T, -target[1].T], axis=-1)
    right_pairs = [(i, i + 1) for i in range(blocks - 1)]
    left_pairs = [(i + 1, i) for i in range(blocks - 1)]
    is_first = position == 0
    is_last = position == blocks - 1

    fwd_buf = jnp.zeros((chunks + 2, members_here, 2 * order, width), jnp.float32)
    bwd_buf = jnp.zeros((chunks + 2, members_here, width, 2 * order), jnp.float32)
    fwd_out = None
    bwd_out = None
    steps = chunks + blocks - 1
    for step in range(steps):
        if step == 0:
            fwd_in = jnp.zeros((members_here, 2 * order, width), jnp.float32)
            bwd_in = jnp.zeros((members_here, width, 2 * order), jnp.float32)
        else:
            fwd_in = lax.ppermute(fwd_out, "tm", right_pairs)
            bwd_in = lax.ppermute(bwd_out, "tm", left_pairs)
        if step < chunks:
            cols = slice(step * width, (step + 1) * width)
            own_cols = jnp.concatenate([unit[:, 0, :, cols], unit[:, 1, :, cols]], axis=-2)
            rows = jnp.broadcast_to(target_dag[None, step * width:(step + 1) * width], bwd_in.shape)
            if step == 0:
                fwd_new = own_cols
            else:
                fwd_new = jnp.where(
                    is_first, own_cols,
                    jnp.einsum("mab,mbw->maw", left_op, fwd_in, precision=HIGH),
                )
            bwd_in = jnp.where(is_last, rows, bwd_in)
        else:
            fwd_new = jnp.einsum("mab,mbw->maw", left_op, fwd_in, precision=HIGH)
        fwd_chunk = jnp.clip(step - position, -1, chunks) + 1
        bwd_chunk = jnp.clip(step - (blocks - 1 - position), -1, chunks) + 1
        fwd_buf = lax.dynamic_update_index_in_dim(fwd_buf, fwd_new, fwd_chunk, 0)
        bwd_buf = lax.dynamic_update_index_in_dim(bwd_buf, bwd_in, bwd_chunk, 0)
        fwd_out = fwd_new
        if step < steps - 1:
            bwd_out = jnp.einsum("mwa,mab->mwb", bwd_in, right_op, precision=HIGH)

    fwd_all = fwd_buf[1:chunks + 1].reshape(chunks, members_here, 2, order, width)
    bwd_all = bwd_buf[1:chunks + 1].reshape(chunks, members_here, width, 2, order)
    parts = jnp.einsum("cmpaw,cmwqb->mpqab", fwd_all, bwd_all, precision=HIGH)
    q_re = parts[:, 0, 0] - parts[:, 1, 1]
    q_im = parts[:, 0, 1] + parts[:, 1, 0]
    eye = jnp.eye(order, dtype=bool)
    over_re = jnp.sum(jnp.where(eye, q_re, 0.0), axis=(-2, -1))
    over_im = jnp.sum(jnp.where(eye, q_im, 0.0), axis=(-2, -1))
    h_re = controls[None, :, 0]
    h_im = controls[None, :, 1]
    s_re = jnp.sum(q_re[:, None] * h_re + q_im[:, None] * h_im, axis=(-2, -1))
    s_im = jnp.sum(q_im[:, None] * h_re - q_re[:, None] * h_im, axis=(-2, -1))
    terms = over_re[:, None] * s_im - over_im[:, None] * s_re
    partial_value = jnp.sum(terms, axis=0, keepdims=True)
    total = butterfly_sum(partial_value, ("sub", "member"))
    member_count = members_here * lax.axis_size("member") * lax.axis_size("sub")
    return total * (2.0 / member_count)


def solution(mesh):
    placed = (P(("group", "member", "sub"), "tm", None, None, None), P(), P("group", None, None))
    return jax.shard_map(
        per_device, mesh=mesh, in_specs=placed, out_specs=P(("group", "tm"), None), check_vma=False
    )
```

```python
import jax
import jax.numpy as jnp
from jax import lax
from jax.sharding import PartitionSpec as P

HIGH = lax.Precision.HIGH
CHUNKS = 2


def block_left(u):
    top = jnp.concatenate([u[:, 0], -u[:, 1]], axis=-1)
    bottom = jnp.concatenate([u[:, 1], u[:, 0]], axis=-1)
    return jnp.concatenate([top, bottom], axis=-2)


def block_right(u):
    top = jnp.concatenate([u[:, 0], u[:, 1]], axis=-1)
    bottom = jnp.concatenate([-u[:, 1], u[:, 0]], axis=-1)
    return jnp.concatenate([top, bottom], axis=-2)


def butterfly_sum(value, axes):
    for axis in axes:
        size = lax.axis_size(axis)
        if size & (size - 1):
            value = lax.psum(value, axis)
            continue
        distance = 1
        while distance < size:
            pairs = [(i, i ^ distance) for i in range(size)]
            value = value + lax.ppermute(value, axis, pairs)
            distance *= 2
    return value


def per_device(slices, controls, target):
    members_here = slices.shape[0]
    order = slices.shape[-1]
    chunks = CHUNKS
    width = order // chunks
    blocks = lax.axis_size("tm")
    position = lax.axis_index("tm")
    unit = slices[:, 0]
    left_op = block_left(unit)
    right_op = block_right(unit)
    target_dag = jnp.concatenate([target[0].T, -target[1].T], axis=-1)
    right_pairs = [(i, i + 1) for i in range(blocks - 1)]
    left_pairs = [(i + 1, i) for i in range(blocks - 1)]
    is_first = position == 0
    is_last = position == blocks - 1

    fwd_buf = jnp.zeros((chunks + 2, members_here, 2 * order, width), jnp.float32)
    bwd_buf = jnp.zeros((chunks + 2, members_here, width, 2 * order), jnp.float32)
    fwd_out = None
    bwd_out = None
    steps = chunks + blocks - 1
    for step in range(steps):
        if step == 0:
            fwd_in = jnp.zeros((members_here, 2 * order, width), jnp.float32)
            bwd_in = jnp.zeros((members_here, width, 2 * order), jnp.float32)
        else:
            fwd_in = lax.ppermute(fwd_out, "tm", right_pairs)
            bwd_in = lax.ppermute(bwd_out, "tm", left_pairs)
        if step < chunks:
            cols = slice(step * width, (step + 1) * width)
            own_cols = jnp.concatenate([unit[:, 0, :, cols], unit[:, 1, :, cols]], axis=-2)
            rows = jnp.broadcast_to(target_dag[None, step * width:(step + 1) * width], bwd_in.shape)
            if step == 0:
                fwd_new = own_cols
            else:
                fwd_new = jnp.where(
                    is_first, own_cols,
                    jnp.einsum("mab,mbw->maw", left_op, fwd_in, precision=HIGH),
                )
            bwd_in = jnp.where(is_last, rows, bwd_in)
        else:
            fwd_new = jnp.einsum("mab,mbw->maw", left_op, fwd_in, precision=HIGH)
        fwd_chunk = jnp.clip(step - position, -1, chunks) + 1
        bwd_chunk = jnp.clip(step - (blocks - 1 - position), -1, chunks) + 1
        fwd_buf = lax.dynamic_update_index_in_dim(fwd_buf, fwd_new, fwd_chunk, 0)
        bwd_buf = lax.dynamic_update_index_in_dim(bwd_buf, bwd_in, bwd_chunk, 0)
        fwd_out = fwd_new
        if step < steps - 1:
            bwd_out = jnp.einsum("mwa,mab->mwb", bwd_in, right_op, precision=HIGH)

    fwd_all = fwd_buf[1:chunks + 1].reshape(chunks, members_here, 2, order, width)
    bwd_all = bwd_buf[1:chunks + 1].reshape(chunks, members_here, width, 2, order)
    parts = jnp.einsum("cmpaw,cmwqb->mpqab", fwd_all, bwd_all, precision=HIGH)
    q_re = parts[:, 0, 0] - parts[:, 1, 1]
    q_im = parts[:, 0, 1] + parts[:, 1, 0]
    eye = jnp.eye(order, dtype=bool)
    over_re = jnp.sum(jnp.where(eye, q_re, 0.0), axis=(-2, -1))
    over_im = jnp.sum(jnp.where(eye, q_im, 0.0), axis=(-2, -1))
    h_re = controls[None, :, 0]
    h_im = controls[None, :, 1]
    s_re = jnp.sum(q_re[:, None] * h_re + q_im[:, None] * h_im, axis=(-2, -1))
    s_im = jnp.sum(q_im[:, None] * h_re - q_re[:, None] * h_im, axis=(-2, -1))
    terms = over_re[:, None] * s_im - over_im[:, None] * s_re
    partial_value = jnp.sum(terms, axis=0, keepdims=True)
    total = butterfly_sum(partial_value, ("sub", "member"))
    member_count = members_here * lax.axis_size("member") * lax.axis_size("sub")
    return total * (2.0 / member_count)


def solution(mesh):
    placed = (P(("group", "member", "sub"), "tm", None, None, None), P(), P("group", None, None))
    return jax.shard_map(
        per_device, mesh=mesh, in_specs=placed, out_specs=P(("group", "tm"), None), check_vma=False
    )
```

```python
import jax
import jax.numpy as jnp
from jax import lax
from jax.sharding import PartitionSpec as P

HIGH = lax.Precision.HIGH
CHUNKS = 2


def block_left(u):
    top = jnp.concatenate([u[:, 0], -u[:, 1]], axis=-1)
    bottom = jnp.concatenate([u[:, 1], u[:, 0]], axis=-1)
    return jnp.concatenate([top, bottom], axis=-2)


def block_right(u):
    top = jnp.concatenate([u[:, 0], u[:, 1]], axis=-1)
    bottom = jnp.concatenate([-u[:, 1], u[:, 0]], axis=-1)
    return jnp.concatenate([top, bottom], axis=-2)


def butterfly_sum(value, axes):
    for axis in axes:
        size = lax.axis_size(axis)
        if size & (size - 1):
            value = lax.psum(value, axis)
            continue
        distance = 1
        while distance < size:
            pairs = [(i, i ^ distance) for i in range(size)]
            value = value + lax.ppermute(value, axis, pairs)
            distance *= 2
    return value


def per_device(slices, controls, target):
    members_here = slices.shape[0]
    order = slices.shape[-1]
    chunks = CHUNKS
    width = order // chunks
    blocks = lax.axis_size("tm")
    position = lax.axis_index("tm")
    unit = slices[:, 0]
    left_op = block_left(unit)
    right_op = block_right(unit)
    target_dag = jnp.concatenate([target[0].T, -target[1].T], axis=-1)
    right_pairs = [(i, i + 1) for i in range(blocks - 1)]
    left_pairs = [(i + 1, i) for i in range(blocks - 1)]
    is_first = position == 0
    is_last = position == blocks - 1

    fwd_steps = []
    bwd_steps = []
    fwd_out = None
    bwd_out = None
    steps = chunks + blocks - 1
    for step in range(steps):
        if step == 0:
            fwd_in = jnp.zeros((members_here, 2 * order, width), jnp.float32)
            bwd_in = jnp.zeros((members_here, width, 2 * order), jnp.float32)
        else:
            fwd_in = lax.ppermute(fwd_out, "tm", right_pairs)
            bwd_in = lax.ppermute(bwd_out, "tm", left_pairs)
        if step < chunks:
            cols = slice(step * width, (step + 1) * width)
            own_cols = jnp.concatenate([unit[:, 0, :, cols], unit[:, 1, :, cols]], axis=-2)
            rows = jnp.broadcast_to(target_dag[None, step * width:(step + 1) * width], bwd_in.shape)
            if step == 0:
                fwd_new = own_cols
            else:
                fwd_new = jnp.where(
                    is_first, own_cols,
                    jnp.einsum("mab,mbw->maw", left_op, fwd_in, precision=HIGH),
                )
            bwd_in = jnp.where(is_last, rows, bwd_in)
        else:
            fwd_new = jnp.einsum("mab,mbw->maw", left_op, fwd_in, precision=HIGH)
        fwd_steps.append(fwd_new)
        bwd_steps.append(bwd_in)
        fwd_out = fwd_new
        if step < steps - 1:
            bwd_out = jnp.einsum("mwa,mab->mwb", bwd_in, right_op, precision=HIGH)

    fwd_all = lax.dynamic_slice_in_dim(jnp.stack(fwd_steps), position, chunks, 0)
    bwd_all = lax.dynamic_slice_in_dim(jnp.stack(bwd_steps), blocks - 1 - position, chunks, 0)
    fwd_all = fwd_all.reshape(chunks, members_here, 2, order, width)
    bwd_all = bwd_all.reshape(chunks, members_here, width, 2, order)
    parts = jnp.einsum("cmpaw,cmwqb->mpqab", fwd_all, bwd_all, precision=HIGH)
    q_re = parts[:, 0, 0] - parts[:, 1, 1]
    q_im = parts[:, 0, 1] + parts[:, 1, 0]
    eye = jnp.eye(order, dtype=bool)
    over_re = jnp.sum(jnp.where(eye, q_re, 0.0), axis=(-2, -1))
    over_im = jnp.sum(jnp.where(eye, q_im, 0.0), axis=(-2, -1))
    h_re = controls[None, :, 0]
    h_im = controls[None, :, 1]
    s_re = jnp.sum(q_re[:, None] * h_re + q_im[:, None] * h_im, axis=(-2, -1))
    s_im = jnp.sum(q_im[:, None] * h_re - q_re[:, None] * h_im, axis=(-2, -1))
    terms = over_re[:, None] * s_im - over_im[:, None] * s_re
    partial_value = jnp.sum(terms, axis=0, keepdims=True)
    total = butterfly_sum(partial_value, ("sub", "member"))
    member_count = members_here * lax.axis_size("member") * lax.axis_size("sub")
    return total * (2.0 / member_count)


def solution(mesh):
    placed = (P(("group", "member", "sub"), "tm", None, None, None), P(), P("group", None, None))
    return jax.shard_map(
        per_device, mesh=mesh, in_specs=placed, out_specs=P(("group", "tm"), None), check_vma=False
    )
```

```python
import jax
import jax.numpy as jnp
from jax import lax
from jax.sharding import PartitionSpec as P

HIGH = lax.Precision.HIGH
CHUNKS = 2


def block_left(u):
    top = jnp.concatenate([u[:, 0], -u[:, 1]], axis=-1)
    bottom = jnp.concatenate([u[:, 1], u[:, 0]], axis=-1)
    return jnp.concatenate([top, bottom], axis=-2)


def block_right(u):
    top = jnp.concatenate([u[:, 0], u[:, 1]], axis=-1)
    bottom = jnp.concatenate([-u[:, 1], u[:, 0]], axis=-1)
    return jnp.concatenate([top, bottom], axis=-2)


def butterfly_sum(value, axes):
    for axis in axes:
        size = lax.axis_size(axis)
        if size & (size - 1):
            value = lax.psum(value, axis)
            continue
        distance = 1
        while distance < size:
            pairs = [(i, i ^ distance) for i in range(size)]
            value = value + lax.ppermute(value, axis, pairs)
            distance *= 2
    return value


def member_sum(value):
    axes = ("member", "sub")
    count = lax.axis_size("member") * lax.axis_size("sub")
    if count != 4:
        return butterfly_sum(value, ("sub", "member"))
    got = [lax.ppermute(value, axes, [(i, i ^ d) for i in range(4)]) for d in (1, 2, 3)]
    return (value + got[0]) + (got[1] + got[2])


def per_device(slices, controls, target):
    members_here = slices.shape[0]
    order = slices.shape[-1]
    chunks = CHUNKS
    width = order // chunks
    blocks = lax.axis_size("tm")
    position = lax.axis_index("tm")
    unit = slices[:, 0]
    left_op = block_left(unit)
    right_op = block_right(unit)
    target_dag = jnp.concatenate([target[0].T, -target[1].T], axis=-1)
    right_pairs = [(i, i + 1) for i in range(blocks - 1)]
    left_pairs = [(i + 1, i) for i in range(blocks - 1)]
    is_first = position == 0
    is_last = position == blocks - 1

    fwd_steps = []
    bwd_steps = []
    fwd_out = None
    bwd_out = None
    steps = chunks + blocks - 1
    for step in range(steps):
        if step == 0:
            fwd_in = jnp.zeros((members_here, width, 2 * order), jnp.float32)
            bwd_in = jnp.zeros((members_here, width, 2 * order), jnp.float32)
        else:
            fwd_in = lax.ppermute(fwd_out, "tm", right_pairs)
            bwd_in = lax.ppermute(bwd_out, "tm", left_pairs)
        if step < chunks:
            cols = slice(step * width, (step + 1) * width)
            own_cols = jnp.swapaxes(
                jnp.concatenate([unit[:, 0, :, cols], unit[:, 1, :, cols]], axis=-2), -1, -2)
            rows = jnp.broadcast_to(target_dag[None, step * width:(step + 1) * width], bwd_in.shape)
            if step == 0:
                fwd_new = own_cols
            else:
                fwd_new = jnp.where(
                    is_first, own_cols,
                    jnp.einsum("mwb,mab->mwa", fwd_in, left_op, precision=HIGH),
                )
            bwd_in = jnp.where(is_last, rows, bwd_in)
        else:
            fwd_new = jnp.einsum("mwb,mab->mwa", fwd_in, left_op, precision=HIGH)
        fwd_steps.append(fwd_new)
        bwd_steps.append(bwd_in)
        fwd_out = fwd_new
        if step < steps - 1:
            bwd_out = jnp.einsum("mwa,mab->mwb", bwd_in, right_op, precision=HIGH)

    fwd_all = lax.dynamic_slice_in_dim(jnp.stack(fwd_steps), position, chunks, 0)
    bwd_all = lax.dynamic_slice_in_dim(jnp.stack(bwd_steps), blocks - 1 - position, chunks, 0)
    fwd_all = fwd_all.reshape(chunks, members_here, width, 2, order)
    bwd_all = bwd_all.reshape(chunks, members_here, width, 2, order)
    parts = jnp.einsum("cmwpa,cmwqb->mpqab", fwd_all, bwd_all, precision=HIGH)
    q_re = parts[:, 0, 0] - parts[:, 1, 1]
    q_im = parts[:, 0, 1] + parts[:, 1, 0]
    eye = jnp.eye(order, dtype=bool)
    over_re = jnp.sum(jnp.where(eye, q_re, 0.0), axis=(-2, -1))
    over_im = jnp.sum(jnp.where(eye, q_im, 0.0), axis=(-2, -1))
    h_re = controls[None, :, 0]
    h_im = controls[None, :, 1]
    s_re = jnp.sum(q_re[:, None] * h_re + q_im[:, None] * h_im, axis=(-2, -1))
    s_im = jnp.sum(q_im[:, None] * h_re - q_re[:, None] * h_im, axis=(-2, -1))
    terms = over_re[:, None] * s_im - over_im[:, None] * s_re
    partial_value = jnp.sum(terms, axis=0, keepdims=True)
    total = member_sum(partial_value)
    member_count = members_here * lax.axis_size("member") * lax.axis_size("sub")
    return total * (2.0 / member_count)


def solution(mesh):
    placed = (P(("group", "member", "sub"), "tm", None, None, None), P(), P("group", None, None))
    return jax.shard_map(
        per_device, mesh=mesh, in_specs=placed, out_specs=P(("group", "tm"), None), check_vma=False
    )
```

```python
import jax
import jax.numpy as jnp
from jax import lax
from jax.sharding import PartitionSpec as P

HIGH = lax.Precision.HIGH
CHUNKS = 2


def block_left(u):
    top = jnp.concatenate([u[:, 0], -u[:, 1]], axis=-1)
    bottom = jnp.concatenate([u[:, 1], u[:, 0]], axis=-1)
    return jnp.concatenate([top, bottom], axis=-2)


def block_right(u):
    top = jnp.concatenate([u[:, 0], u[:, 1]], axis=-1)
    bottom = jnp.concatenate([-u[:, 1], u[:, 0]], axis=-1)
    return jnp.concatenate([top, bottom], axis=-2)


def gauss_ops(u):
    return jnp.stack([u[:, 0], u[:, 1], u[:, 0] + u[:, 1]], axis=1)


def gauss_left(ops, x):
    order = ops.shape[-1]
    x_re, x_im = x[:, :order], x[:, order:]
    rhs = jnp.stack([x_re, x_im, x_re + x_im], axis=1)
    p = jnp.einsum("mtab,mtbw->mtaw", ops, rhs, precision=HIGH)
    return jnp.concatenate([p[:, 0] - p[:, 1], p[:, 2] - p[:, 0] - p[:, 1]], axis=-2)


def gauss_right(x, ops):
    order = ops.shape[-1]
    x_re, x_im = x[..., :order], x[..., order:]
    lhs = jnp.stack([x_re, x_im, x_re + x_im], axis=1)
    p = jnp.einsum("mtwa,mtab->mtwb", lhs, ops, precision=HIGH)
    return jnp.concatenate([p[:, 0] - p[:, 1], p[:, 2] - p[:, 0] - p[:, 1]], axis=-1)


def butterfly_sum(value, axes):
    for axis in axes:
        size = lax.axis_size(axis)
        if size & (size - 1):
            value = lax.psum(value, axis)
            continue
        distance = 1
        while distance < size:
            pairs = [(i, i ^ distance) for i in range(size)]
            value = value + lax.ppermute(value, axis, pairs)
            distance *= 2
    return value


def per_device(slices, controls, target):
    members_here = slices.shape[0]
    order = slices.shape[-1]
    chunks = CHUNKS
    width = order // chunks
    blocks = lax.axis_size("tm")
    position = lax.axis_index("tm")
    unit = slices[:, 0]
    ops = gauss_ops(unit)
    target_dag = jnp.concatenate([target[0].T, -target[1].T], axis=-1)
    right_pairs = [(i, i + 1) for i in range(blocks - 1)]
    left_pairs = [(i + 1, i) for i in range(blocks - 1)]
    is_first = position == 0
    is_last = position == blocks - 1

    fwd_steps = []
    bwd_steps = []
    fwd_out = None
    bwd_out = None
    steps = chunks + blocks - 1
    for step in range(steps):
        if step == 0:
            fwd_in = jnp.zeros((members_here, 2 * order, width), jnp.float32)
            bwd_in = jnp.zeros((members_here, width, 2 * order), jnp.float32)
        else:
            fwd_in = lax.ppermute(fwd_out, "tm", right_pairs)
            bwd_in = lax.ppermute(bwd_out, "tm", left_pairs)
        if step < chunks:
            cols = slice(step * width, (step + 1) * width)
            own_cols = jnp.concatenate([unit[:, 0, :, cols], unit[:, 1, :, cols]], axis=-2)
            rows = jnp.broadcast_to(target_dag[None, step * width:(step + 1) * width], bwd_in.shape)
            if step == 0:
                fwd_new = own_cols
            else:
                fwd_new = jnp.where(
                    is_first, own_cols,
                    gauss_left(ops, fwd_in),
                )
            bwd_in = jnp.where(is_last, rows, bwd_in)
        else:
            fwd_new = gauss_left(ops, fwd_in)
        fwd_steps.append(fwd_new)
        bwd_steps.append(bwd_in)
        fwd_out = fwd_new
        if step < steps - 1:
            bwd_out = gauss_right(bwd_in, ops)

    fwd_all = lax.dynamic_slice_in_dim(jnp.stack(fwd_steps), position, chunks, 0)
    bwd_all = lax.dynamic_slice_in_dim(jnp.stack(bwd_steps), blocks - 1 - position, chunks, 0)
    fwd_all = fwd_all.reshape(chunks, members_here, 2, order, width)
    bwd_all = bwd_all.reshape(chunks, members_here, width, 2, order)
    parts = jnp.einsum("cmpaw,cmwqb->mpqab", fwd_all, bwd_all, precision=HIGH)
    q_re = parts[:, 0, 0] - parts[:, 1, 1]
    q_im = parts[:, 0, 1] + parts[:, 1, 0]
    eye = jnp.eye(order, dtype=bool)
    over_re = jnp.sum(jnp.where(eye, q_re, 0.0), axis=(-2, -1))
    over_im = jnp.sum(jnp.where(eye, q_im, 0.0), axis=(-2, -1))
    h_re = controls[None, :, 0]
    h_im = controls[None, :, 1]
    s_re = jnp.sum(q_re[:, None] * h_re + q_im[:, None] * h_im, axis=(-2, -1))
    s_im = jnp.sum(q_im[:, None] * h_re - q_re[:, None] * h_im, axis=(-2, -1))
    terms = over_re[:, None] * s_im - over_im[:, None] * s_re
    partial_value = jnp.sum(terms, axis=0, keepdims=True)
    total = butterfly_sum(partial_value, ("sub", "member"))
    member_count = members_here * lax.axis_size("member") * lax.axis_size("sub")
    return total * (2.0 / member_count)


def solution(mesh):
    placed = (P(("group", "member", "sub"), "tm", None, None, None), P(), P("group", None, None))
    return jax.shard_map(
        per_device, mesh=mesh, in_specs=placed, out_specs=P(("group", "tm"), None), check_vma=False
    )
```

```python
import jax
import jax.numpy as jnp
from jax import lax
from jax.sharding import PartitionSpec as P

HIGH = lax.Precision.HIGH
CHUNKS = 2


def block_left(u):
    top = jnp.concatenate([u[:, 0], -u[:, 1]], axis=-1)
    bottom = jnp.concatenate([u[:, 1], u[:, 0]], axis=-1)
    return jnp.concatenate([top, bottom], axis=-2)


def block_right(u):
    top = jnp.concatenate([u[:, 0], u[:, 1]], axis=-1)
    bottom = jnp.concatenate([-u[:, 1], u[:, 0]], axis=-1)
    return jnp.concatenate([top, bottom], axis=-2)


def gauss_ops(u):
    return jnp.stack([u[:, 0], u[:, 1], u[:, 0] + u[:, 1]], axis=1)


def gauss_left(ops, x):
    order = ops.shape[-1]
    x_re, x_im = x[:, :order], x[:, order:]
    rhs = jnp.stack([x_re, x_im, x_re + x_im], axis=1)
    p = jnp.einsum("mtab,mtbw->mtaw", ops, rhs, precision=HIGH)
    return jnp.concatenate([p[:, 0] - p[:, 1], p[:, 2] - p[:, 0] - p[:, 1]], axis=-2)


def gauss_right(x, ops):
    order = ops.shape[-1]
    x_re, x_im = x[..., :order], x[..., order:]
    lhs = jnp.stack([x_re, x_im, x_re + x_im], axis=1)
    p = jnp.einsum("mtwa,mtab->mtwb", lhs, ops, precision=HIGH)
    return jnp.concatenate([p[:, 0] - p[:, 1], p[:, 2] - p[:, 0] - p[:, 1]], axis=-1)


def butterfly_sum(value, axes):
    for axis in axes:
        size = lax.axis_size(axis)
        if size & (size - 1):
            value = lax.psum(value, axis)
            continue
        distance = 1
        while distance < size:
            pairs = [(i, i ^ distance) for i in range(size)]
            value = value + lax.ppermute(value, axis, pairs)
            distance *= 2
    return value


def per_device(slices, controls, target):
    members_here = slices.shape[0]
    order = slices.shape[-1]
    chunks = CHUNKS
    width = order // chunks
    blocks = lax.axis_size("tm")
    position = lax.axis_index("tm")
    unit = slices[:, 0]
    ops = gauss_ops(unit)
    target_dag = jnp.concatenate([target[0].T, -target[1].T], axis=-1)
    is_first = position == 0
    is_last = position == blocks - 1

    fwd_steps = []
    bwd_steps = []
    fwd_out = None
    bwd_out = None
    steps = chunks + blocks - 1
    for step in range(steps):
        if step == 0:
            fwd_in = jnp.zeros((members_here, 2 * order, width), jnp.float32)
            bwd_in = jnp.zeros((members_here, width, 2 * order), jnp.float32)
        else:
            fwd_pairs = [(i, i + 1) for i in range(max(0, step - chunks), min(blocks - 1, step))]
            bwd_pairs = [(j, j - 1) for j in range(max(1, blocks - step), min(blocks, blocks - step + chunks))]
            fwd_in = lax.ppermute(fwd_out, "tm", fwd_pairs)
            bwd_in = lax.ppermute(bwd_out, "tm", bwd_pairs)
        if step < chunks:
            cols = slice(step * width, (step + 1) * width)
            own_cols = jnp.concatenate([unit[:, 0, :, cols], unit[:, 1, :, cols]], axis=-2)
            rows = jnp.broadcast_to(target_dag[None, step * width:(step + 1) * width], bwd_in.shape)
            if step == 0:
                fwd_new = own_cols
            else:
                fwd_new = jnp.where(
                    is_first, own_cols,
                    gauss_left(ops, fwd_in),
                )
            bwd_in = jnp.where(is_last, rows, bwd_in)
        else:
            fwd_new = gauss_left(ops, fwd_in)
        fwd_steps.append(fwd_new)
        bwd_steps.append(bwd_in)
        fwd_out = fwd_new
        if step < steps - 1:
            bwd_out = gauss_right(bwd_in, ops)

    fwd_all = lax.dynamic_slice_in_dim(jnp.stack(fwd_steps), position, chunks, 0)
    bwd_all = lax.dynamic_slice_in_dim(jnp.stack(bwd_steps), blocks - 1 - position, chunks, 0)
    fwd_all = fwd_all.reshape(chunks, members_here, 2, order, width)
    bwd_all = bwd_all.reshape(chunks, members_here, width, 2, order)
    parts = jnp.einsum("cmpaw,cmwqb->mpqab", fwd_all, bwd_all, precision=HIGH)
    q_re = parts[:, 0, 0] - parts[:, 1, 1]
    q_im = parts[:, 0, 1] + parts[:, 1, 0]
    eye = jnp.eye(order, dtype=bool)
    over_re = jnp.sum(jnp.where(eye, q_re, 0.0), axis=(-2, -1))
    over_im = jnp.sum(jnp.where(eye, q_im, 0.0), axis=(-2, -1))
    h_re = controls[None, :, 0]
    h_im = controls[None, :, 1]
    s_re = jnp.sum(q_re[:, None] * h_re + q_im[:, None] * h_im, axis=(-2, -1))
    s_im = jnp.sum(q_im[:, None] * h_re - q_re[:, None] * h_im, axis=(-2, -1))
    terms = over_re[:, None] * s_im - over_im[:, None] * s_re
    partial_value = jnp.sum(terms, axis=0, keepdims=True)
    total = butterfly_sum(partial_value, ("sub", "member"))
    member_count = members_here * lax.axis_size("member") * lax.axis_size("sub")
    return total * (2.0 / member_count)


def solution(mesh):
    placed = (P(("group", "member", "sub"), "tm", None, None, None), P(), P("group", None, None))
    return jax.shard_map(
        per_device, mesh=mesh, in_specs=placed, out_specs=P(("group", "tm"), None), check_vma=False
    )
```
